256 devices in a mesh: ctx: 32 (over y, x, core), exp: 8 (over z).
Axes of the slice: x: 4, y: 4, z: 8, core: 2. Of those that a mesh axis runs over, the one named last changes fastest.
Arguments:
- ssm_input: bfloat16 [4096, 4096], P('ctx', 'exp'), may hold values from -6 to 6
- gate_input: bfloat16 [4096, 4096], P('ctx', 'exp'), may hold values from -6 to 6
- key_proj: bfloat16 [4096, 128], P('ctx'), may hold values from -4 to 4
- query_proj: bfloat16 [4096, 128], P('ctx'), may hold values from -4 to 4
- step_size: float32 [4096, 64], P('ctx', 'exp'), may hold values from 0 to 1, as said below
- decay_rate: float32 [64], P('exp'), may hold values from 0.5 to 1.5
- head_gain: float32 [4096], P('exp'), may hold values from 0.5 to 1.5
- residual: bfloat16 [4096, 4096], P('ctx', 'exp'), may hold values from -33 to 33
- ffn_gain: float32 [4096], replicated, may hold values from 0.5 to 1.5
- gate_weight: bfloat16 [8, 4096, 12288], P('exp', None, 'ctx'), may hold values from -0.09375 to 0.09375
- up_weight: bfloat16 [8, 4096, 12288], P('exp', None, 'ctx'), may hold values from -0.09375 to 0.09375
- down_weight: bfloat16 [8, 12288, 4096], P('exp', 'ctx'), may hold values from -0.0546875 to 0.0546875
- expert_ids: int32 [4096, 2], P('ctx'), may hold values from 0 to 7, all different within a row; in each aligned block of 128 rows (0 to 127, 128 to 255, ...) at most 48 rows name the same one
- route_weight: float32 [4096, 2], P('ctx'), may hold values from 0.5 to 2
Outputs:
- block_out: bfloat16 [4096, 4096], P('ctx', 'exp')
- expert_out: bfloat16 [4096, 4096], P('ctx', 'exp')
The draws below stay inside these ranges and needn't reach their ends.
Inputs may be any that keep to these rules, and one draw needn't show every extreme that they name: `step_size`: step sizes are positive. `expert_ids`: the two experts of a token differ. In each aligned block of 128 rows (the tokens of one shard) no expert is named by more than 48 rows, and in some block one expert is named by exactly 48 rows.
All inputs are finite; a program needn't handle non-finite values.
Results may differ from the reference program's by a relative error of at most 0.022.
Values may be sent and summed in bfloat16 or wider, within the bound.
No kernel may reach another device: no remote copies, remote signals or barrier semaphores. Data moves between devices by JAX's collectives and lax.ppermute only.
A program may use at most 128 MiB of HBM per device.

```python
import math
import jax
import jax.numpy as jnp
import numpy as np
from jax import lax

D = 4096
HEADS = 64
NSTATE = 128
FF = 12288
L_DEV = 128
CONTEXT_LENGTH = 4096
EXPERTS = 8
CAP = 48


def draw_step_size(key, part):
    gradual_prng_seed, coarse_prng_seed, cluster_prng_seed = jax.random.split(key, 3)
    slow_share = 0.5
    slow_heads = jax.random.uniform(gradual_prng_seed, (HEADS,)) < slow_share
    background_intensity = jnp.where(slow_heads, 0.3 / CONTEXT_LENGTH, 1.0 / 40.0)
    perturbation_magnitude = jnp.exp(jax.random.uniform(coarse_prng_seed, (CONTEXT_LENGTH, HEADS), minval=-0.69, maxval=0.69))
    cluster_location = jax.random.randint(cluster_prng_seed, (2,), 0, CONTEXT_LENGTH)
    element_location = jnp.arange(CONTEXT_LENGTH)
    cluster_occurrences = jnp.any(element_location[:, None] == cluster_location[None, :], axis=1).astype(jnp.float32) * 0.45
    return (background_intensity[None, :] * perturbation_magnitude + cluster_occurrences[:, None]).astype(jnp.float32)


def draw_residual(key, part):
    key_column, key_row, key_entry = jax.random.split(key, 3)
    column_ramp = 1.0 + 2.0 * jnp.arange(D, dtype=jnp.float32) / D
    column_scale = column_ramp * jnp.exp(jax.random.uniform(key_column, (D,), minval=0.0, maxval=math.log(4.0)))
    row_scale = jnp.exp(jax.random.uniform(key_row, (CONTEXT_LENGTH, 1), minval=0.0, maxval=math.log(3.0)))
    entries = jax.random.truncated_normal(key_entry, -6.0, 6.0, (CONTEXT_LENGTH, D))
    return (0.15 * entries * row_scale * column_scale[None, :]).astype(jnp.bfloat16)


def shard_levels(own_key, dims, cuts, low, largest):
    def one(position, shards_of):
        heights = jax.random.uniform(jax.random.fold_in(jax.random.fold_in(own_key, 6), position), (shards_of,), jnp.float32, low / len(cuts), largest / len(cuts))
        return jnp.repeat(jnp.exp(heights), dims[position] // shards_of).reshape((-1,) + (1,) * (len(dims) - position - 1))

    factor_of = one(*cuts[0])
    for cut in cuts[1:]:
        factor_of = factor_of * one(*cut)
    return factor_of


def assign_block(rng, own, number, rows, count, top, limit, lean):
    sequence = jax.random.permutation(rng, count)
    packed, usual = portions_of(count, rows * top, limit, lean, True), portions_of(count, rows * top, limit, lean, False)
    places = jnp.arange(count)

    def named(lengths, turn):
        used = int((lengths > 0).sum())
        fixed = max(1, used // 4)
        moved = fixed + (places - fixed + turn * (used - fixed)) % max(1, count - fixed)
        return jnp.zeros((count,), jnp.int32).at[sequence[jnp.where(places < fixed, places, moved)]].set(jnp.asarray(lengths, jnp.int32))

    lengths = jnp.where(number % 4 == 0, named(packed, number // 4), named(usual, number - number // 4 - 1))
    mixed = jax.random.permutation(jax.random.fold_in(own, 3), count)
    giver, sink = mixed[0:count // 2 * 2:2], mixed[1:count // 2 * 2:2]
    margin = jnp.minimum(lengths[giver] - 1, limit - lengths[sink]) // 2
    margin = jnp.where((giver == sequence[0]) | (sink == sequence[0]) | (lengths[sink] == 0), 0, jnp.maximum(margin, 0))
    moved = jax.random.randint(jax.random.fold_in(own, 4), (count // 2,), 0, 1 << 20) % (margin + 1)
    lengths = lengths.at[giver].add(-moved).at[sink].add(moved)
    items = jnp.searchsorted(jnp.cumsum(lengths), jnp.arange(rows * top), side="right").astype(jnp.int32)
    table = items.reshape(top, rows).T
    table = table[jax.random.permutation(jax.random.fold_in(own, 1), rows)]
    turn = jax.random.randint(jax.random.fold_in(own, 2), (rows, 1), 0, top)
    return jnp.take_along_axis(table, (jnp.arange(top)[None, :] + turn) % top, axis=1)


def portions_of(amount, total, bound, skew, full):
    loads = [(1 << 20) // math.isqrt(grade ** skew) + 1 for grade in range(1, amount + 1)]
    largest = bound if full else min(bound, max(-(-total // amount), total * loads[0] // sum(loads)))
    least = 1 if total - largest >= amount - 1 else 0
    counts, rest = [largest] + [least] * (amount - 1), total - largest - least * (amount - 1)
    while rest > 0:
        candidates = [i for i in range(1, amount) if counts[i] < largest] or [i for i in range(1, amount) if counts[i] < bound]
        mass, remaining = sum([loads[i] for i in candidates]), rest
        for i in candidates:
            addition = min(bound - counts[i], max(1, remaining * loads[i] // mass), rest)
            counts[i] = counts[i] + addition
            rest = rest - addition
    return np.array(counts)


def scatter_about(rng, dims, width, limit, shards=(), kind=jnp.bfloat16):
    gain = shard_levels(rng, dims, shards, -0.22, 0.18) if shards else 1.0
    drawn = jax.random.normal(rng, dims, jnp.float32) * width * gain
    return jnp.minimum(jnp.maximum(drawn, -limit), limit).astype(kind)


def setup_inputs(seed: int = 0) -> dict:
    arg_keys = jax.random.split(jax.random.key(seed), 15)
    ssm_input = scatter_about(arg_keys[0], (CONTEXT_LENGTH, D), 1.0, 6.0, ((0, 32), (1, 8)))
    gate_input = scatter_about(arg_keys[1], (CONTEXT_LENGTH, D), 1.0, 6.0, ((0, 32), (1, 8)))
    key_proj = scatter_about(arg_keys[2], (CONTEXT_LENGTH, NSTATE), 0.3, 4.0, ((0, 32),))
    query_proj = scatter_about(arg_keys[3], (CONTEXT_LENGTH, NSTATE), 0.3, 4.0, ((0, 32),))
    step_size = draw_step_size(jax.random.fold_in(arg_keys[14], 71), 0)
    decay_rate = jnp.clip(jnp.exp(math.log(1.5) - 1.0986123 * jax.random.uniform(arg_keys[5], (HEADS,), jnp.float32) ** shard_levels(arg_keys[5], (HEADS,), ((0, 8),), -0.2, 0.2)), 0.5, 1.5)
    head_gain = jnp.clip(1.0 + 0.1 * jax.random.normal(arg_keys[6], (D,), jnp.float32), 0.5, 1.5)
    residual = draw_residual(jax.random.fold_in(arg_keys[14], 71), 0)
    ffn_gain = jnp.clip(1.0 + 0.1 * jax.random.normal(arg_keys[8], (D,), jnp.float32), 0.5, 1.5)
    gate_weight = scatter_about(arg_keys[9], (EXPERTS, D, FF), D ** -0.5, 0.09375, ((0, 8), (2, 32)))
    up_weight = scatter_about(arg_keys[10], (EXPERTS, D, FF), D ** -0.5, 0.09375, ((0, 8), (2, 32)))
    down_weight = scatter_about(arg_keys[11], (EXPERTS, FF, D), FF ** -0.5, 0.0546875, ((0, 8), (1, 32)))
    expert_ids_keys = jax.random.split(jax.random.fold_in(arg_keys[12], 1), CONTEXT_LENGTH // L_DEV)
    expert_ids_turns = jax.random.permutation(jax.random.fold_in(arg_keys[12], 3), CONTEXT_LENGTH // L_DEV)
    expert_ids = jax.vmap(lambda own, number: assign_block(jax.random.fold_in(arg_keys[12], 2), own, number, L_DEV, EXPERTS, 2, CAP, 2))(expert_ids_keys, expert_ids_turns).reshape((CONTEXT_LENGTH, 2))
    route_weight = jnp.clip(jnp.exp(math.log(2.0) - 1.3862944 * jax.random.uniform(arg_keys[13], (CONTEXT_LENGTH, 2), jnp.float32) ** shard_levels(arg_keys[13], (CONTEXT_LENGTH, 2), ((0, 32),), -0.2, 0.2)), 0.5, 2.0)
    return {"ssm_input": ssm_input, "gate_input": gate_input, "key_proj": key_proj, "query_proj": query_proj, "step_size": step_size, "decay_rate": decay_rate, "head_gain": head_gain, "residual": residual, "ffn_gain": ffn_gain, "gate_weight": gate_weight, "up_weight": up_weight, "down_weight": down_weight, "expert_ids": expert_ids, "route_weight": route_weight}


precise = lax.Precision.HIGHEST

def local_block(ssm_piece, key_piece, query_piece, step_piece, decay_rate, head_count):
    row_count = ssm_piece.shape[0]
    head_width = ssm_piece.shape[1] // head_count
    values = ssm_piece.astype(jnp.float32).reshape(row_count, head_count, head_width)
    key_vals = key_piece.astype(jnp.float32)
    queries = query_piece.astype(jnp.float32)
    log_steps = -step_piece * decay_rate[None, :]
    running = jnp.cumsum(log_steps, axis=0)
    scores = jnp.dot(queries, key_vals.T, precision=precise)
    causal = (jnp.arange(row_count)[:, None] >= jnp.arange(row_count)[None, :])[:, :, None]
    spacing = running[:, None, :] - running[None, :, :]
    decays = jnp.where(causal, jnp.exp(jnp.where(causal, spacing, 0.0)), 0.0)
    within = jnp.einsum('tsh,ts,shp->thp', decays, scores, values, precision=precise)
    overall = running[-1]
    fading = jnp.exp(overall[None, :] - running)
    states = jnp.einsum('sh,shp,sn->hpn', fading, values, key_vals, precision=precise)
    return (within, running, overall, states)

def route_tables(expert_ids, route_weight, experts, capacity):
    matched = expert_ids[None, :, :] == experts[:, None, None]
    member = jnp.any(matched, axis=2).astype(jnp.int32)
    gate_sum = lax.optimization_barrier(jnp.sum(jnp.where(matched, route_weight[None, :, :], 0.0), axis=2))
    slot_index = jnp.cumsum(member, axis=1) - 1
    positions = jnp.arange(capacity, dtype=jnp.int32)
    routing = ((slot_index[:, None, :] == positions[None, :, None]) & (member[:, None, :] > 0)).astype(jnp.float32)
    slot_weight = jnp.einsum('nkt,nt->nk', routing, gate_sum, precision=precise)
    return (routing, slot_weight)

def reference(ssm_input, gate_input, key_proj, query_proj, step_size, decay_rate, head_gain, residual, ffn_gain, gate_weight, up_weight, down_weight, expert_ids, route_weight):
    blocks = CONTEXT_LENGTH // L_DEV
    head_width = D // HEADS

    def state_step(incoming, block_in):
        within, running, overall, states = local_block(block_in[0], block_in[1], block_in[2], block_in[3], decay_rate, HEADS)
        carried = jnp.einsum('th,hpn,tn->thp', jnp.exp(running), incoming, block_in[2].astype(jnp.float32), precision=precise)
        following = jnp.exp(overall)[:, None, None] * incoming + states
        return (following, within + carried)
    initial = jnp.zeros((HEADS, head_width, NSTATE), jnp.float32)
    pieces = (ssm_input.reshape(blocks, L_DEV, D), key_proj.reshape(blocks, L_DEV, NSTATE), query_proj.reshape(blocks, L_DEV, NSTATE), step_size.reshape(blocks, L_DEV, HEADS))
    ignored, outputs = lax.scan(state_step, initial, pieces)
    mixer_out = outputs.reshape(CONTEXT_LENGTH, HEADS, head_width)
    gated_out = mixer_out * jax.nn.silu(gate_input.astype(jnp.float32)).reshape(CONTEXT_LENGTH, HEADS, head_width)
    inv_rms = lax.rsqrt(lax.optimization_barrier(jnp.mean(gated_out * gated_out, axis=2, keepdims=True)) + 1e-05)
    normed = (gated_out * inv_rms).reshape(CONTEXT_LENGTH, D) * head_gain[None, :]
    block_out = (residual.astype(jnp.float32) + normed).astype(jnp.bfloat16)
    widened = block_out.astype(jnp.float32)
    ffn_input = (widened * lax.rsqrt(lax.optimization_barrier(jnp.mean(widened * widened, axis=1, keepdims=True)) + 1e-06) * ffn_gain[None, :]).astype(jnp.bfloat16)
    slice_width = FF // blocks
    shard_ids = expert_ids.reshape(blocks, L_DEV, 2)
    shard_weight = route_weight.reshape(blocks, L_DEV, 2)
    shard_in = ffn_input.astype(jnp.float32).reshape(blocks, L_DEV, D)

    def one_expert(combined, expert):

        def per_shard(shard_rows, shard_gates):
            return route_tables(shard_rows, shard_gates, jnp.reshape(expert, (1,)), CAP)
        tables, weights = jax.vmap(per_shard)(shard_ids, shard_weight)
        tables = tables[:, 0]
        weights = weights[:, 0]
        chosen = jnp.einsum('ckt,ctd->ckd', tables, shard_in, precision=precise).astype(jnp.bfloat16).reshape(blocks * CAP, D)
        gate_all = gate_weight[expert]
        up_all = up_weight[expert]
        down_all = down_weight[expert]

        def one_slice(running_sum, slice_index):
            offset = slice_index * slice_width
            gate_part = lax.dynamic_slice_in_dim(gate_all, offset, slice_width, 1)
            up_part = lax.dynamic_slice_in_dim(up_all, offset, slice_width, 1)
            down_part = lax.dynamic_slice_in_dim(down_all, offset, slice_width, 0)
            hidden = (jax.nn.silu(jnp.dot(chosen, gate_part, preferred_element_type=jnp.float32)) * jnp.dot(chosen, up_part, preferred_element_type=jnp.float32)).astype(jnp.bfloat16)
            partial_value = jnp.dot(hidden, down_part, preferred_element_type=jnp.float32).astype(jnp.bfloat16)
            return (running_sum + lax.optimization_barrier(partial_value).astype(jnp.float32), None)
        summed, unused = lax.scan(one_slice, jnp.zeros((blocks * CAP, D), jnp.float32), jnp.arange(blocks, dtype=jnp.int32))
        result = lax.optimization_barrier(summed.astype(jnp.bfloat16)).astype(jnp.float32).reshape(blocks, CAP, D)
        returned = jnp.einsum('ckt,ck,ckd->ctd', tables, weights, result, precision=precise)
        return (combined + returned.reshape(CONTEXT_LENGTH, D), None)
    combined, unused = lax.scan(one_expert, jnp.zeros((CONTEXT_LENGTH, D), jnp.float32), jnp.arange(EXPERTS, dtype=jnp.int32))
    return (block_out, combined.astype(jnp.bfloat16))
```

```python
import jax
import jax.numpy as jnp
from jax import lax
from jax.sharding import Mesh, PartitionSpec as P

precise = lax.Precision.HIGHEST
CTX = ("chip", "core")


def local_block(ssm_piece, key_piece, query_piece, step_piece, decay_rate, head_count):
    row_count = ssm_piece.shape[0]
    head_width = ssm_piece.shape[1] // head_count
    values = ssm_piece.astype(jnp.float32).reshape(row_count, head_count, head_width)
    key_vals = key_piece.astype(jnp.float32)
    queries = query_piece.astype(jnp.float32)
    log_steps = -step_piece * decay_rate[None, :]
    running = jnp.cumsum(log_steps, axis=0)
    scores = jnp.dot(queries, key_vals.T, precision=precise)
    causal = (jnp.arange(row_count)[:, None] >= jnp.arange(row_count)[None, :])[:, :, None]
    spacing = running[:, None, :] - running[None, :, :]
    decays = jnp.where(causal, jnp.exp(jnp.where(causal, spacing, 0.0)), 0.0)
    within = jnp.einsum("tsh,ts,shp->thp", decays, scores, values, precision=precise)
    overall = running[-1]
    fading = jnp.exp(overall[None, :] - running)
    states = jnp.einsum("sh,shp,sn->hpn", fading, values, key_vals, precision=precise)
    return (within, running, overall, states)


def route_tables(expert_ids, route_weight, experts, capacity):
    matched = expert_ids[None, :, :] == experts[:, None, None]
    member = jnp.any(matched, axis=2).astype(jnp.int32)
    gate_sum = jnp.sum(jnp.where(matched, route_weight[None, :, :], 0.0), axis=2)
    slot_index = jnp.cumsum(member, axis=1) - 1
    positions = jnp.arange(capacity, dtype=jnp.int32)
    routing = (
        (slot_index[:, None, :] == positions[None, :, None]) & (member[:, None, :] > 0)
    ).astype(jnp.float32)
    return (routing, gate_sum)


def carried_state(overall, states):
    head_count, head_width, nstate = states.shape
    flat = states.astype(jnp.bfloat16).reshape(head_count * head_width, nstate)
    high = overall.astype(jnp.bfloat16)
    low = (overall - high.astype(jnp.float32)).astype(jnp.bfloat16)
    extra = jnp.zeros((8, nstate), jnp.bfloat16)
    extra = extra.at[0, :head_count].set(high).at[1, :head_count].set(low)
    packed = jnp.concatenate([flat, extra], axis=0)
    chips = lax.axis_size("chip")
    cores = lax.axis_size("core")
    by_chip = lax.all_gather(packed, "chip")
    everything = lax.all_gather(by_chip, "core")
    shards = chips * cores
    everything = everything.reshape(shards, packed.shape[0], nstate)
    core_of = jnp.arange(shards, dtype=jnp.int32) // chips
    chip_of = jnp.arange(shards, dtype=jnp.int32) % chips
    shard_of = chip_of * cores + core_of
    me = lax.axis_index("chip") * cores + lax.axis_index("core")
    rows = head_count * head_width
    decay_all = (
        everything[:, rows, :head_count].astype(jnp.float32)
        + everything[:, rows + 1, :head_count].astype(jnp.float32)
    )
    between = (shard_of[:, None] < shard_of[None, :]) & (shard_of[None, :] < me)
    spans = jnp.sum(jnp.where(between[:, :, None], decay_all[None, :, :], 0.0), axis=1)
    weight = jnp.where((shard_of < me)[:, None], jnp.exp(spans), 0.0)
    gathered = everything[:, :rows, :].astype(jnp.float32).reshape(
        shards, head_count, head_width, nstate
    )
    return jnp.einsum("kh,khpn->hpn", weight, gathered, precision=precise)


def on_device(
    ssm_input,
    gate_input,
    key_proj,
    query_proj,
    step_size,
    decay_rate,
    head_gain,
    residual,
    ffn_gain,
    gate_weight,
    up_weight,
    down_weight,
    expert_ids,
    route_weight,
):
    head_count = step_size.shape[1]
    row_count, channels = ssm_input.shape
    head_width = channels // head_count
    within, running, overall, states = local_block(
        ssm_input, key_proj, query_proj, step_size, decay_rate, head_count
    )
    before = carried_state(overall, states)
    carried = jnp.einsum(
        "th,hpn,tn->thp",
        jnp.exp(running),
        before,
        query_proj.astype(jnp.float32),
        precision=precise,
    )
    mixer_out = within + carried
    gated_out = mixer_out * jax.nn.silu(gate_input.astype(jnp.float32)).reshape(
        row_count, head_count, head_width
    )
    inv_rms = lax.rsqrt(jnp.mean(gated_out * gated_out, axis=2, keepdims=True) + 1e-05)
    normed = (gated_out * inv_rms).reshape(row_count, channels) * head_gain[None, :]
    block_out = (residual.astype(jnp.float32) + normed).astype(jnp.bfloat16)

    exp_count = lax.axis_size("exp")
    capacity = 3 * row_count // exp_count
    tables, gate_sum = route_tables(
        expert_ids, route_weight, jnp.arange(exp_count, dtype=jnp.int32), capacity
    )
    picked = jnp.einsum(
        "ekt,td->ekd",
        tables.astype(jnp.bfloat16),
        block_out,
        preferred_element_type=jnp.float32,
    ).astype(jnp.bfloat16)
    arrived = lax.all_to_all(picked, "exp", 0, 0)
    own_rows = jnp.transpose(arrived, (1, 0, 2)).reshape(capacity, exp_count * channels)
    widened = own_rows.astype(jnp.float32)
    chosen = (
        widened
        * lax.rsqrt(jnp.mean(widened * widened, axis=1, keepdims=True) + 1e-06)
        * ffn_gain[None, :]
    ).astype(jnp.bfloat16)

    gate_here = gate_weight[0]
    up_here = up_weight[0]
    down_here = down_weight[0]
    token_piece = lax.all_gather(
        lax.all_gather(chosen, "chip", axis=0, tiled=True), "core", axis=0, tiled=True
    )
    gate_proj = jnp.dot(token_piece, gate_here, preferred_element_type=jnp.float32)
    up_proj = jnp.dot(token_piece, up_here, preferred_element_type=jnp.float32)
    hidden = (jax.nn.silu(gate_proj) * up_proj).astype(jnp.bfloat16)
    partial_value = jnp.dot(hidden, down_here, preferred_element_type=jnp.float32).astype(
        jnp.bfloat16
    )
    summed = lax.psum_scatter(
        lax.psum_scatter(partial_value, "core", scatter_dimension=0, tiled=True),
        "chip",
        scatter_dimension=0,
        tiled=True,
    )
    outgoing = jnp.transpose(summed.reshape(capacity, exp_count, channels), (1, 0, 2))
    returned = lax.all_to_all(outgoing, "exp", 0, 0)
    weights = tables * gate_sum[:, None, :]
    expert_out = jnp.einsum(
        "ekt,ekd->td", weights, returned.astype(jnp.float32), precision=precise
    ).astype(jnp.bfloat16)
    return (block_out, expert_out)


def solution(mesh):
    ctx_size, exp_size = mesh.devices.shape
    split = Mesh(mesh.devices.reshape(ctx_size // 2, 2, exp_size), ("chip", "core", "exp"))
    placed = (
        P(CTX, "exp"),
        P(CTX, "exp"),
        P(CTX, None),
        P(CTX, None),
        P(CTX, "exp"),
        P("exp"),
        P("exp"),
        P(CTX, "exp"),
        P(),
        P("exp", None, CTX),
        P("exp", None, CTX),
        P("exp", CTX, None),
        P(CTX, None),
        P(CTX, None),
    )
    return jax.shard_map(
        on_device,
        mesh=split,
        in_specs=placed,
        out_specs=(P(CTX, "exp"), P(CTX, "exp")),
        check_vma=False,
    )
```

```python
import jax
import jax.numpy as jnp
from jax import lax
from jax.sharding import PartitionSpec as P

precise = lax.Precision.HIGHEST


def local_block(ssm_piece, key_piece, query_piece, step_piece, decay_rate, head_count):
    row_count = ssm_piece.shape[0]
    head_width = ssm_piece.shape[1] // head_count
    values = ssm_piece.astype(jnp.float32).reshape(row_count, head_count, head_width)
    key_vals = key_piece.astype(jnp.float32)
    queries = query_piece.astype(jnp.float32)
    log_steps = -step_piece * decay_rate[None, :]
    running = jnp.cumsum(log_steps, axis=0)
    scores = jnp.dot(queries, key_vals.T, precision=precise)
    causal = (jnp.arange(row_count)[:, None] >= jnp.arange(row_count)[None, :])[:, :, None]
    spacing = running[:, None, :] - running[None, :, :]
    decays = jnp.where(causal, jnp.exp(jnp.where(causal, spacing, 0.0)), 0.0)
    within = jnp.einsum("tsh,ts,shp->thp", decays, scores, values, precision=precise)
    overall = running[-1]
    fading = jnp.exp(overall[None, :] - running)
    states = jnp.einsum("sh,shp,sn->hpn", fading, values, key_vals, precision=precise)
    return (within, running, overall, states)


def route_tables(expert_ids, route_weight, experts, capacity):
    matched = expert_ids[None, :, :] == experts[:, None, None]
    member = jnp.any(matched, axis=2).astype(jnp.int32)
    gate_sum = jnp.sum(jnp.where(matched, route_weight[None, :, :], 0.0), axis=2)
    slot_index = jnp.cumsum(member, axis=1) - 1
    positions = jnp.arange(capacity, dtype=jnp.int32)
    routing = (
        (slot_index[:, None, :] == positions[None, :, None]) & (member[:, None, :] > 0)
    ).astype(jnp.float32)
    return (routing, gate_sum)


def carried_state(overall, states):
    head_count, head_width, nstate = states.shape
    shards = lax.axis_size("ctx")
    rows = head_count * head_width
    extra = jnp.zeros((8, nstate), jnp.float32).at[0, :head_count].set(overall)
    packed = jnp.concatenate([states.reshape(rows, nstate), extra], axis=0)

    def shift(value, distance):
        pairs = [(i, i + distance) for i in range(shards - distance)]
        return lax.ppermute(value, "ctx", pairs)

    packed = shift(packed, 1)
    distance = 1
    while distance < shards:
        earlier = shift(packed, distance)
        decay = packed[rows, :head_count]
        joined = (
            jnp.exp(decay)[:, None, None] * earlier[:rows].reshape(head_count, head_width, nstate)
            + packed[:rows].reshape(head_count, head_width, nstate)
        )
        packed = jnp.concatenate(
            [joined.reshape(rows, nstate), earlier[rows:] + packed[rows:]], axis=0
        )
        distance *= 2
    return packed[:rows].reshape(head_count, head_width, nstate)


def on_device(
    ssm_input,
    gate_input,
    key_proj,
    query_proj,
    step_size,
    decay_rate,
    head_gain,
    residual,
    ffn_gain,
    gate_weight,
    up_weight,
    down_weight,
    expert_ids,
    route_weight,
):
    head_count = step_size.shape[1]
    row_count, channels = ssm_input.shape
    head_width = channels // head_count
    within, running, overall, states = local_block(
        ssm_input, key_proj, query_proj, step_size, decay_rate, head_count
    )
    before = carried_state(overall, states)
    carried = jnp.einsum(
        "th,hpn,tn->thp",
        jnp.exp(running),
        before,
        query_proj.astype(jnp.float32),
        precision=precise,
    )
    mixer_out = within + carried
    gated_out = mixer_out * jax.nn.silu(gate_input.astype(jnp.float32)).reshape(
        row_count, head_count, head_width
    )
    inv_rms = lax.rsqrt(jnp.mean(gated_out * gated_out, axis=2, keepdims=True) + 1e-05)
    normed = (gated_out * inv_rms).reshape(row_count, channels) * head_gain[None, :]
    block_out = (residual.astype(jnp.float32) + normed).astype(jnp.bfloat16)

    exp_count = lax.axis_size("exp")
    capacity = 3 * row_count // exp_count
    tables, gate_sum = route_tables(
        expert_ids, route_weight, jnp.arange(exp_count, dtype=jnp.int32), capacity
    )
    picked = jnp.einsum(
        "ekt,td->ekd",
        tables.astype(jnp.bfloat16),
        block_out,
        preferred_element_type=jnp.float32,
    ).astype(jnp.bfloat16)
    arrived = lax.all_to_all(picked, "exp", 0, 0)
    own_rows = jnp.transpose(arrived, (1, 0, 2)).reshape(capacity, exp_count * channels)
    widened = own_rows.astype(jnp.float32)
    chosen = (
        widened
        * lax.rsqrt(jnp.mean(widened * widened, axis=1, keepdims=True) + 1e-06)
        * ffn_gain[None, :]
    ).astype(jnp.bfloat16)

    gate_here = gate_weight[0]
    up_here = up_weight[0]
    down_here = down_weight[0]
    token_piece = lax.all_gather(chosen, "ctx", axis=0, tiled=True)
    gate_proj = jnp.dot(token_piece, gate_here, preferred_element_type=jnp.float32)
    up_proj = jnp.dot(token_piece, up_here, preferred_element_type=jnp.float32)
    hidden = (jax.nn.silu(gate_proj) * up_proj).astype(jnp.bfloat16)
    partial_value = jnp.dot(hidden, down_here, preferred_element_type=jnp.float32).astype(
        jnp.bfloat16
    )
    summed = lax.psum_scatter(partial_value, "ctx", scatter_dimension=0, tiled=True)
    outgoing = jnp.transpose(summed.reshape(capacity, exp_count, channels), (1, 0, 2))
    returned = lax.all_to_all(outgoing, "exp", 0, 0)
    weights = tables * gate_sum[:, None, :]
    expert_out = jnp.einsum(
        "ekt,ekd->td", weights, returned.astype(jnp.float32), precision=precise
    ).astype(jnp.bfloat16)
    return (block_out, expert_out)


def solution(mesh):
    placed = (
        P("ctx", "exp"),
        P("ctx", "exp"),
        P("ctx", None),
        P("ctx", None),
        P("ctx", "exp"),
        P("exp"),
        P("exp"),
        P("ctx", "exp"),
        P(),
        P("exp", None, "ctx"),
        P("exp", None, "ctx"),
        P("exp", "ctx", None),
        P("ctx", None),
        P("ctx", None),
    )
    return jax.shard_map(
        on_device,
        mesh=mesh,
        in_specs=placed,
        out_specs=(P("ctx", "exp"), P("ctx", "exp")),
        check_vma=False,
    )
```

```python
import jax
import jax.numpy as jnp
from jax import lax
from jax.sharding import PartitionSpec as P

precise = lax.Precision.HIGHEST


def local_block(ssm_piece, key_piece, query_piece, step_piece, decay_rate, head_count):
    row_count = ssm_piece.shape[0]
    head_width = ssm_piece.shape[1] // head_count
    values = ssm_piece.astype(jnp.float32).reshape(row_count, head_count, head_width)
    key_vals = key_piece.astype(jnp.float32)
    queries = query_piece.astype(jnp.float32)
    log_steps = -step_piece * decay_rate[None, :]
    running = jnp.cumsum(log_steps, axis=0)
    scores = jnp.dot(queries, key_vals.T, precision=precise)
    causal = (jnp.arange(row_count)[:, None] >= jnp.arange(row_count)[None, :])[:, :, None]
    spacing = running[:, None, :] - running[None, :, :]
    decays = jnp.where(causal, jnp.exp(jnp.where(causal, spacing, 0.0)), 0.0)
    within = jnp.einsum("tsh,ts,shp->thp", decays, scores, values, precision=precise)
    overall = running[-1]
    fading = jnp.exp(overall[None, :] - running)
    states = jnp.einsum("sh,shp,sn->hpn", fading, values, key_vals, precision=precise)
    return (within, running, overall, states)


def route_tables(expert_ids, route_weight, experts, capacity):
    matched = expert_ids[None, :, :] == experts[:, None, None]
    member = jnp.any(matched, axis=2).astype(jnp.int32)
    gate_sum = jnp.sum(jnp.where(matched, route_weight[None, :, :], 0.0), axis=2)
    slot_index = jnp.cumsum(member, axis=1) - 1
    positions = jnp.arange(capacity, dtype=jnp.int32)
    routing = (
        (slot_index[:, None, :] == positions[None, :, None]) & (member[:, None, :] > 0)
    ).astype(jnp.float32)
    return (routing, gate_sum)


def carried_state(overall, states):
    head_count, head_width, nstate = states.shape
    rows = head_count * head_width
    high = overall.astype(jnp.bfloat16)
    low = (overall - high.astype(jnp.float32)).astype(jnp.bfloat16)
    extra = jnp.zeros((8, nstate), jnp.bfloat16)
    extra = extra.at[0, :head_count].set(high).at[1, :head_count].set(low)
    packed = jnp.concatenate([states.astype(jnp.bfloat16).reshape(rows, nstate), extra], axis=0)
    everything = lax.all_gather(packed, "ctx")
    shards = everything.shape[0]
    me = lax.axis_index("ctx")
    decay_all = (
        everything[:, rows, :head_count].astype(jnp.float32)
        + everything[:, rows + 1, :head_count].astype(jnp.float32)
    )
    shard_of = jnp.arange(shards, dtype=jnp.int32)
    between = (shard_of[:, None] < shard_of[None, :]) & (shard_of[None, :] < me)
    spans = jnp.sum(jnp.where(between[:, :, None], decay_all[None, :, :], 0.0), axis=1)
    weight = jnp.where((shard_of < me)[:, None], jnp.exp(spans), 0.0)
    gathered = everything[:, :rows, :].astype(jnp.float32).reshape(
        shards, head_count, head_width, nstate
    )
    return jnp.sum(weight[:, :, None, None] * gathered, axis=0)


def on_device(
    ssm_input,
    gate_input,
    key_proj,
    query_proj,
    step_size,
    decay_rate,
    head_gain,
    residual,
    ffn_gain,
    gate_weight,
    up_weight,
    down_weight,
    expert_ids,
    route_weight,
):
    head_count = step_size.shape[1]
    row_count, channels = ssm_input.shape
    head_width = channels // head_count
    within, running, overall, states = local_block(
        ssm_input, key_proj, query_proj, step_size, decay_rate, head_count
    )
    before = carried_state(overall, states)
    carried = jnp.einsum(
        "th,hpn,tn->thp",
        jnp.exp(running),
        before,
        query_proj.astype(jnp.float32),
        precision=precise,
    )
    mixer_out = within + carried
    gated_out = mixer_out * jax.nn.silu(gate_input.astype(jnp.float32)).reshape(
        row_count, head_count, head_width
    )
    inv_rms = lax.rsqrt(jnp.mean(gated_out * gated_out, axis=2, keepdims=True) + 1e-05)
    normed = (gated_out * inv_rms).reshape(row_count, channels) * head_gain[None, :]
    block_out = (residual.astype(jnp.float32) + normed).astype(jnp.bfloat16)

    exp_count = lax.axis_size("exp")
    capacity = 3 * row_count // exp_count
    tables, gate_sum = route_tables(
        expert_ids, route_weight, jnp.arange(exp_count, dtype=jnp.int32), capacity
    )
    picked = jnp.einsum(
        "ekt,td->ekd",
        tables.astype(jnp.bfloat16),
        block_out,
        preferred_element_type=jnp.float32,
    ).astype(jnp.bfloat16)
    arrived = lax.all_to_all(picked, "exp", 0, 0)
    own_rows = jnp.transpose(arrived, (1, 0, 2)).reshape(capacity, exp_count * channels)
    widened = own_rows.astype(jnp.float32)
    chosen = (
        widened
        * lax.rsqrt(jnp.mean(widened * widened, axis=1, keepdims=True) + 1e-06)
        * ffn_gain[None, :]
    ).astype(jnp.bfloat16)

    gate_here = gate_weight[0]
    up_here = up_weight[0]
    down_here = down_weight[0]
    token_piece = lax.all_gather(chosen, "ctx", axis=0, tiled=True)
    gate_proj = jnp.dot(token_piece, gate_here, preferred_element_type=jnp.float32)
    up_proj = jnp.dot(token_piece, up_here, preferred_element_type=jnp.float32)
    hidden = (jax.nn.silu(gate_proj) * up_proj).astype(jnp.bfloat16)
    partial_value = jnp.dot(hidden, down_here, preferred_element_type=jnp.float32).astype(
        jnp.bfloat16
    )
    summed = lax.psum_scatter(partial_value, "ctx", scatter_dimension=0, tiled=True)
    outgoing = jnp.transpose(summed.reshape(capacity, exp_count, channels), (1, 0, 2))
    returned = lax.all_to_all(outgoing, "exp", 0, 0)
    weights = tables * gate_sum[:, None, :]
    expert_out = jnp.einsum(
        "ekt,ekd->td", weights, returned.astype(jnp.float32), precision=precise
    ).astype(jnp.bfloat16)
    return (block_out, expert_out)


def solution(mesh):
    placed = (
        P("ctx", "exp"),
        P("ctx", "exp"),
        P("ctx", None),
        P("ctx", None),
        P("ctx", "exp"),
        P("exp"),
        P("exp"),
        P("ctx", "exp"),
        P(),
        P("exp", None, "ctx"),
        P("exp", None, "ctx"),
        P("exp", "ctx", None),
        P("ctx", None),
        P("ctx", None),
    )
    return jax.shard_map(
        on_device,
        mesh=mesh,
        in_specs=placed,
        out_specs=(P("ctx", "exp"), P("ctx", "exp")),
        check_vma=False,
    )
```

```python
import jax
import jax.numpy as jnp
from jax import lax
from jax.sharding import PartitionSpec as P

precise = lax.Precision.HIGHEST


def local_block(ssm_piece, key_piece, query_piece, step_piece, decay_rate, head_count):
    row_count = ssm_piece.shape[0]
    head_width = ssm_piece.shape[1] // head_count
    values = ssm_piece.astype(jnp.float32).reshape(row_count, head_count, head_width)
    key_vals = key_piece.astype(jnp.float32)
    queries = query_piece.astype(jnp.float32)
    log_steps = -step_piece * decay_rate[None, :]
    running = jnp.cumsum(log_steps, axis=0)
    scores = jnp.dot(queries, key_vals.T, precision=precise)
    causal = (jnp.arange(row_count)[:, None] >= jnp.arange(row_count)[None, :])[:, :, None]
    spacing = running[:, None, :] - running[None, :, :]
    decays = jnp.where(causal, jnp.exp(jnp.where(causal, spacing, 0.0)), 0.0)
    within = jnp.einsum("tsh,ts,shp->thp", decays, scores, values, precision=precise)
    overall = running[-1]
    fading = jnp.exp(overall[None, :] - running)
    states = jnp.einsum("sh,shp,sn->hpn", fading, values, key_vals, precision=precise)
    return (within, running, overall, states)


def route_tables(expert_ids, route_weight, experts, capacity):
    matched = expert_ids[None, :, :] == experts[:, None, None]
    member = jnp.any(matched, axis=2).astype(jnp.int32)
    gate_sum = jnp.sum(jnp.where(matched, route_weight[None, :, :], 0.0), axis=2)
    slot_index = jnp.cumsum(member, axis=1) - 1
    positions = jnp.arange(capacity, dtype=jnp.int32)
    routing = (
        (slot_index[:, None, :] == positions[None, :, None]) & (member[:, None, :] > 0)
    ).astype(jnp.float32)
    return (routing, gate_sum)


def carried_state(overall, states):
    head_count, head_width, nstate = states.shape
    rows = head_count * head_width
    high = overall.astype(jnp.bfloat16)
    low = (overall - high.astype(jnp.float32)).astype(jnp.bfloat16)
    extra = jnp.zeros((8, nstate), jnp.bfloat16)
    extra = extra.at[0, :head_count].set(high).at[1, :head_count].set(low)
    packed = jnp.concatenate([states.astype(jnp.bfloat16).reshape(rows, nstate), extra], axis=0)
    everything = lax.all_gather(packed, "ctx")
    shards = everything.shape[0]
    me = lax.axis_index("ctx")
    decay_all = (
        everything[:, rows, :head_count].astype(jnp.float32)
        + everything[:, rows + 1, :head_count].astype(jnp.float32)
    )
    shard_of = jnp.arange(shards, dtype=jnp.int32)
    between = (shard_of[:, None] < shard_of[None, :]) & (shard_of[None, :] < me)
    spans = jnp.sum(jnp.where(between[:, :, None], decay_all[None, :, :], 0.0), axis=1)
    weight = jnp.where((shard_of < me)[:, None], jnp.exp(spans), 0.0)
    gathered = everything[:, :rows, :].astype(jnp.float32).reshape(
        shards, head_count, head_width, nstate
    )
    return jnp.sum(weight[:, :, None, None] * gathered, axis=0)


def exchange(blocks, axis):
    count = blocks.shape[0]
    me = lax.axis_index(axis)
    received = [lax.dynamic_index_in_dim(blocks, me, 0, keepdims=False)]
    for step in range(1, count):
        piece = lax.dynamic_index_in_dim(blocks, (me + step) % count, 0, keepdims=False)
        pairs = [(i, (i + step) % count) for i in range(count)]
        received.append(lax.ppermute(piece, axis, pairs))
    return jnp.stack(received)


def on_device(
    ssm_input,
    gate_input,
    key_proj,
    query_proj,
    step_size,
    decay_rate,
    head_gain,
    residual,
    ffn_gain,
    gate_weight,
    up_weight,
    down_weight,
    expert_ids,
    route_weight,
):
    head_count = step_size.shape[1]
    row_count, channels = ssm_input.shape
    head_width = channels // head_count
    within, running, overall, states = local_block(
        ssm_input, key_proj, query_proj, step_size, decay_rate, head_count
    )
    before = carried_state(overall, states)
    carried = jnp.einsum(
        "th,hpn,tn->thp",
        jnp.exp(running),
        before,
        query_proj.astype(jnp.float32),
        precision=precise,
    )
    mixer_out = within + carried
    gated_out = mixer_out * jax.nn.silu(gate_input.astype(jnp.float32)).reshape(
        row_count, head_count, head_width
    )
    inv_rms = lax.rsqrt(jnp.mean(gated_out * gated_out, axis=2, keepdims=True) + 1e-05)
    normed = (gated_out * inv_rms).reshape(row_count, channels) * head_gain[None, :]
    block_out = (residual.astype(jnp.float32) + normed).astype(jnp.bfloat16)

    exp_count = lax.axis_size("exp")
    capacity = 3 * row_count // exp_count
    tables, gate_sum = route_tables(
        expert_ids, route_weight, jnp.arange(exp_count, dtype=jnp.int32), capacity
    )
    picked = jnp.einsum(
        "ekt,td->ekd",
        tables.astype(jnp.bfloat16),
        block_out,
        preferred_element_type=jnp.float32,
    ).astype(jnp.bfloat16)
    me = lax.axis_index("exp")
    sources = (me - jnp.arange(exp_count, dtype=jnp.int32)) % exp_count
    arrived = jnp.take(exchange(picked, "exp"), (me - jnp.arange(exp_count)) % exp_count, axis=0)
    own_rows = jnp.transpose(arrived, (1, 0, 2)).reshape(capacity, exp_count * channels)
    widened = own_rows.astype(jnp.float32)
    chosen = (
        widened
        * lax.rsqrt(jnp.mean(widened * widened, axis=1, keepdims=True) + 1e-06)
        * ffn_gain[None, :]
    ).astype(jnp.bfloat16)

    gate_here = gate_weight[0]
    up_here = up_weight[0]
    down_here = down_weight[0]
    token_piece = lax.all_gather(chosen, "ctx", axis=0, tiled=True)
    gate_proj = jnp.dot(token_piece, gate_here, preferred_element_type=jnp.float32)
    up_proj = jnp.dot(token_piece, up_here, preferred_element_type=jnp.float32)
    hidden = (jax.nn.silu(gate_proj) * up_proj).astype(jnp.bfloat16)
    partial_value = jnp.dot(hidden, down_here, preferred_element_type=jnp.float32).astype(
        jnp.bfloat16
    )
    summed = lax.psum_scatter(partial_value, "ctx", scatter_dimension=0, tiled=True)
    outgoing = jnp.transpose(summed.reshape(capacity, exp_count, channels), (1, 0, 2))
    returned = exchange(outgoing, "exp")
    weights = jnp.take(tables * gate_sum[:, None, :], sources, axis=0)
    expert_out = jnp.einsum(
        "ekt,ekd->td", weights, returned.astype(jnp.float32), precision=precise
    ).astype(jnp.bfloat16)
    return (block_out, expert_out)


def solution(mesh):
    placed = (
        P("ctx", "exp"),
        P("ctx", "exp"),
        P("ctx", None),
        P("ctx", None),
        P("ctx", "exp"),
        P("exp"),
        P("exp"),
        P("ctx", "exp"),
        P(),
        P("exp", None, "ctx"),
        P("exp", None, "ctx"),
        P("exp", "ctx", None),
        P("ctx", None),
        P("ctx", None),
    )
    return jax.shard_map(
        on_device,
        mesh=mesh,
        in_specs=placed,
        out_specs=(P("ctx", "exp"), P("ctx", "exp")),
        check_vma=False,
    )
```

```python
import jax
import jax.numpy as jnp
from jax import lax
from jax.sharding import Mesh, PartitionSpec as P

precise = lax.Precision.HIGHEST
CTX = ("chip", "core")


def local_block(ssm_piece, key_piece, query_piece, step_piece, decay_rate, head_count):
    row_count = ssm_piece.shape[0]
    head_width = ssm_piece.shape[1] // head_count
    values = ssm_piece.astype(jnp.float32).reshape(row_count, head_count, head_width)
    key_vals = key_piece.astype(jnp.float32)
    queries = query_piece.astype(jnp.float32)
    log_steps = -step_piece * decay_rate[None, :]
    running = jnp.cumsum(log_steps, axis=0)
    scores = jnp.dot(queries, key_vals.T, precision=precise)
    causal = (jnp.arange(row_count)[:, None] >= jnp.arange(row_count)[None, :])[:, :, None]
    spacing = running[:, None, :] - running[None, :, :]
    decays = jnp.where(causal, jnp.exp(jnp.where(causal, spacing, 0.0)), 0.0)
    within = jnp.einsum("tsh,ts,shp->thp", decays, scores, values, precision=precise)
    overall = running[-1]
    fading = jnp.exp(overall[None, :] - running)
    states = jnp.einsum("sh,shp,sn->hpn", fading, values, key_vals, precision=precise)
    return (within, running, overall, states)


def route_tables(expert_ids, route_weight, experts, capacity):
    matched = expert_ids[None, :, :] == experts[:, None, None]
    member = jnp.any(matched, axis=2).astype(jnp.int32)
    gate_sum = jnp.sum(jnp.where(matched, route_weight[None, :, :], 0.0), axis=2)
    slot_index = jnp.cumsum(member, axis=1) - 1
    positions = jnp.arange(capacity, dtype=jnp.int32)
    routing = (
        (slot_index[:, None, :] == positions[None, :, None]) & (member[:, None, :] > 0)
    ).astype(jnp.float32)
    return (routing, gate_sum)


def carried_state(overall, states):
    head_count, head_width, nstate = states.shape
    rows = head_count * head_width
    high = overall.astype(jnp.bfloat16)
    low = (overall - high.astype(jnp.float32)).astype(jnp.bfloat16)
    extra = jnp.zeros((8, nstate), jnp.bfloat16)
    extra = extra.at[0, :head_count].set(high).at[1, :head_count].set(low)
    packed = jnp.concatenate([states.astype(jnp.bfloat16).reshape(rows, nstate), extra], axis=0)
    everything = lax.all_gather(packed, CTX)
    shards = everything.shape[0]
    me = lax.axis_index(CTX)
    decay_all = (
        everything[:, rows, :head_count].astype(jnp.float32)
        + everything[:, rows + 1, :head_count].astype(jnp.float32)
    )
    shard_of = jnp.arange(shards, dtype=jnp.int32)
    between = (shard_of[:, None] < shard_of[None, :]) & (shard_of[None, :] < me)
    spans = jnp.sum(jnp.where(between[:, :, None], decay_all[None, :, :], 0.0), axis=1)
    weight = jnp.where((shard_of < me)[:, None], jnp.exp(spans), 0.0)
    gathered = everything[:, :rows, :].astype(jnp.float32).reshape(
        shards, head_count, head_width, nstate
    )
    return jnp.sum(weight[:, :, None, None] * gathered, axis=0)


def on_device(
    ssm_input,
    gate_input,
    key_proj,
    query_proj,
    step_size,
    decay_rate,
    head_gain,
    residual,
    ffn_gain,
    gate_weight,
    up_weight,
    down_weight,
    expert_ids,
    route_weight,
):
    head_count = step_size.shape[1]
    row_count, channels = ssm_input.shape
    head_width = channels // head_count
    within, running, overall, states = local_block(
        ssm_input, key_proj, query_proj, step_size, decay_rate, head_count
    )
    before = carried_state(overall, states)
    carried = jnp.einsum(
        "th,hpn,tn->thp",
        jnp.exp(running),
        before,
        query_proj.astype(jnp.float32),
        precision=precise,
    )
    mixer_out = within + carried
    gated_out = mixer_out * jax.nn.silu(gate_input.astype(jnp.float32)).reshape(
        row_count, head_count, head_width
    )
    inv_rms = lax.rsqrt(jnp.mean(gated_out * gated_out, axis=2, keepdims=True) + 1e-05)
    normed = (gated_out * inv_rms).reshape(row_count, channels) * head_gain[None, :]
    block_out = (residual.astype(jnp.float32) + normed).astype(jnp.bfloat16)

    exp_count = lax.axis_size("exp")
    capacity = 3 * row_count // exp_count
    tables, gate_sum = route_tables(
        expert_ids, route_weight, jnp.arange(exp_count, dtype=jnp.int32), capacity
    )
    picked = jnp.einsum(
        "ekt,td->ekd",
        tables.astype(jnp.bfloat16),
        block_out,
        preferred_element_type=jnp.float32,
    ).astype(jnp.bfloat16)
    arrived = lax.all_to_all(picked, "exp", 0, 0)
    own_rows = jnp.transpose(arrived, (1, 0, 2)).reshape(capacity, exp_count * channels)
    widened = own_rows.astype(jnp.float32)
    chosen = (
        widened
        * lax.rsqrt(jnp.mean(widened * widened, axis=1, keepdims=True) + 1e-06)
        * ffn_gain[None, :]
    ).astype(jnp.bfloat16)

    gate_here = gate_weight[0]
    up_here = up_weight[0]
    down_here = down_weight[0]
    token_piece = lax.all_gather(chosen, CTX, axis=0, tiled=True)
    gate_proj = jnp.dot(token_piece, gate_here, preferred_element_type=jnp.float32)
    up_proj = jnp.dot(token_piece, up_here, preferred_element_type=jnp.float32)
    hidden = (jax.nn.silu(gate_proj) * up_proj).astype(jnp.bfloat16)
    chips = lax.axis_size("chip")
    core = lax.axis_index("core")
    by_core = hidden.reshape(chips, 2, capacity, hidden.shape[-1])

    def rows_of(which):
        picked_rows = lax.dynamic_index_in_dim(by_core, which, 1, keepdims=False)
        return picked_rows.reshape(chips * capacity, hidden.shape[-1])

    other_part = jnp.dot(rows_of(1 - core), down_here, preferred_element_type=jnp.float32)
    moved = lax.ppermute(other_part.astype(jnp.bfloat16), "core", [(0, 1), (1, 0)])
    own_part = jnp.dot(rows_of(core), down_here, preferred_element_type=jnp.float32)
    pair_sum = (own_part.astype(jnp.bfloat16).astype(jnp.float32) + moved.astype(jnp.float32)).astype(
        jnp.bfloat16
    )
    summed = lax.psum_scatter(pair_sum, "chip", scatter_dimension=0, tiled=True)
    outgoing = jnp.transpose(summed.reshape(capacity, exp_count, channels), (1, 0, 2))
    returned = lax.all_to_all(outgoing, "exp", 0, 0)
    weights = tables * gate_sum[:, None, :]
    expert_out = jnp.einsum(
        "ekt,ekd->td", weights, returned.astype(jnp.float32), precision=precise
    ).astype(jnp.bfloat16)
    return (block_out, expert_out)


def solution(mesh):
    ctx_size, exp_size = mesh.devices.shape
    split = Mesh(mesh.devices.reshape(ctx_size // 2, 2, exp_size), ("chip", "core", "exp"))
    placed = (
        P(CTX, "exp"),
        P(CTX, "exp"),
        P(CTX, None),
        P(CTX, None),
        P(CTX, "exp"),
        P("exp"),
        P("exp"),
        P(CTX, "exp"),
        P(),
        P("exp", None, CTX),
        P("exp", None, CTX),
        P("exp", CTX, None),
        P(CTX, None),
        P(CTX, None),
    )
    return jax.shard_map(
        on_device,
        mesh=split,
        in_specs=placed,
        out_specs=(P(CTX, "exp"), P(CTX, "exp")),
        check_vma=False,
    )
```

```python
import jax
import jax.numpy as jnp
from jax import lax
from jax.sharding import Mesh, PartitionSpec as P

precise = lax.Precision.HIGHEST
CTX = ("chip", "core")


def local_block(ssm_piece, key_piece, query_piece, step_piece, decay_rate, head_count):
    row_count = ssm_piece.shape[0]
    head_width = ssm_piece.shape[1] // head_count
    values = ssm_piece.astype(jnp.float32).reshape(row_count, head_count, head_width)
    key_vals = key_piece.astype(jnp.float32)
    queries = query_piece.astype(jnp.float32)
    log_steps = -step_piece * decay_rate[None, :]
    running = jnp.cumsum(log_steps, axis=0)
    scores = jnp.dot(queries, key_vals.T, precision=precise)
    causal = (jnp.arange(row_count)[:, None] >= jnp.arange(row_count)[None, :])[:, :, None]
    spacing = running[:, None, :] - running[None, :, :]
    decays = jnp.where(causal, jnp.exp(jnp.where(causal, spacing, 0.0)), 0.0)
    within = jnp.einsum("tsh,ts,shp->thp", decays, scores, values, precision=precise)
    overall = running[-1]
    fading = jnp.exp(overall[None, :] - running)
    states = jnp.einsum("sh,shp,sn->hpn", fading, values, key_vals, precision=precise)
    return (within, running, overall, states)


def route_tables(expert_ids, route_weight, experts, capacity):
    matched = expert_ids[None, :, :] == experts[:, None, None]
    member = jnp.any(matched, axis=2).astype(jnp.int32)
    gate_sum = jnp.sum(jnp.where(matched, route_weight[None, :, :], 0.0), axis=2)
    slot_index = jnp.cumsum(member, axis=1) - 1
    positions = jnp.arange(capacity, dtype=jnp.int32)
    routing = (
        (slot_index[:, None, :] == positions[None, :, None]) & (member[:, None, :] > 0)
    ).astype(jnp.float32)
    return (routing, gate_sum)


def carried_state(overall, states):
    head_count, head_width, nstate = states.shape
    rows = head_count * head_width
    high = overall.astype(jnp.bfloat16)
    low = (overall - high.astype(jnp.float32)).astype(jnp.bfloat16)
    extra = jnp.zeros((8, nstate), jnp.bfloat16)
    extra = extra.at[0, :head_count].set(high).at[1, :head_count].set(low)
    packed = jnp.concatenate([states.astype(jnp.bfloat16).reshape(rows, nstate), extra], axis=0)
    everything = lax.all_gather(packed, CTX)
    shards = everything.shape[0]
    me = lax.axis_index(CTX)
    decay_all = (
        everything[:, rows, :head_count].astype(jnp.float32)
        + everything[:, rows + 1, :head_count].astype(jnp.float32)
    )
    shard_of = jnp.arange(shards, dtype=jnp.int32)
    between = (shard_of[:, None] < shard_of[None, :]) & (shard_of[None, :] < me)
    spans = jnp.sum(jnp.where(between[:, :, None], decay_all[None, :, :], 0.0), axis=1)
    weight = jnp.where((shard_of < me)[:, None], jnp.exp(spans), 0.0)
    gathered = everything[:, :rows, :].astype(jnp.float32).reshape(
        shards, head_count, head_width, nstate
    )
    return jnp.sum(weight[:, :, None, None] * gathered, axis=0)


def on_device(
    ssm_input,
    gate_input,
    key_proj,
    query_proj,
    step_size,
    decay_rate,
    head_gain,
    residual,
    ffn_gain,
    gate_weight,
    up_weight,
    down_weight,
    expert_ids,
    route_weight,
):
    head_count = step_size.shape[1]
    row_count, channels = ssm_input.shape
    head_width = channels // head_count
    within, running, overall, states = local_block(
        ssm_input, key_proj, query_proj, step_size, decay_rate, head_count
    )
    before = carried_state(overall, states)
    carried = jnp.einsum(
        "th,hpn,tn->thp",
        jnp.exp(running),
        before,
        query_proj.astype(jnp.float32),
        precision=precise,
    )
    mixer_out = within + carried
    gated_out = mixer_out * jax.nn.silu(gate_input.astype(jnp.float32)).reshape(
        row_count, head_count, head_width
    )
    inv_rms = lax.rsqrt(jnp.mean(gated_out * gated_out, axis=2, keepdims=True) + 1e-05)
    normed = (gated_out * inv_rms).reshape(row_count, channels) * head_gain[None, :]
    block_out = (residual.astype(jnp.float32) + normed).astype(jnp.bfloat16)

    exp_count = lax.axis_size("exp")
    capacity = 3 * row_count // exp_count
    tables, gate_sum = route_tables(
        expert_ids, route_weight, jnp.arange(exp_count, dtype=jnp.int32), capacity
    )
    picked = jnp.einsum(
        "ekt,td->ekd",
        tables.astype(jnp.bfloat16),
        block_out,
        preferred_element_type=jnp.float32,
    ).astype(jnp.bfloat16)
    arrived = lax.all_to_all(picked, "exp", 0, 0)
    own_rows = jnp.transpose(arrived, (1, 0, 2)).reshape(capacity, exp_count * channels)
    widened = own_rows.astype(jnp.float32)
    chosen = (
        widened
        * lax.rsqrt(jnp.mean(widened * widened, axis=1, keepdims=True) + 1e-06)
        * ffn_gain[None, :]
    ).astype(jnp.bfloat16)

    gate_here = gate_weight[0]
    up_here = up_weight[0]
    down_here = down_weight[0]
    token_piece = lax.all_gather(chosen, CTX, axis=0, tiled=True)
    gate_proj = jnp.dot(token_piece, gate_here, preferred_element_type=jnp.float32)
    up_proj = jnp.dot(token_piece, up_here, preferred_element_type=jnp.float32)
    hidden = (jax.nn.silu(gate_proj) * up_proj).astype(jnp.bfloat16)
    chips = lax.axis_size("chip")
    core = lax.axis_index("core")
    by_core = hidden.reshape(chips, 2, capacity, hidden.shape[-1])

    def rows_of(which):
        picked_rows = lax.dynamic_index_in_dim(by_core, which, 1, keepdims=False)
        return picked_rows.reshape(chips * capacity, hidden.shape[-1])

    other_part = jnp.dot(rows_of(1 - core), down_here, preferred_element_type=jnp.float32)
    moved = lax.ppermute(other_part.astype(jnp.bfloat16), "core", [(0, 1), (1, 0)])
    own_part = jnp.dot(rows_of(core), down_here, preferred_element_type=jnp.float32)
    own_part = lax.optimization_barrier(own_part.astype(jnp.bfloat16))
    pair_sum = (own_part.astype(jnp.float32) + moved.astype(jnp.float32)).astype(jnp.bfloat16)
    summed = lax.psum_scatter(pair_sum, "chip", scatter_dimension=0, tiled=True)
    outgoing = jnp.transpose(summed.reshape(capacity, exp_count, channels), (1, 0, 2))
    returned = lax.all_to_all(outgoing, "exp", 0, 0)
    weights = tables * gate_sum[:, None, :]
    expert_out = jnp.einsum(
        "ekt,ekd->td", weights, returned.astype(jnp.float32), precision=precise
    ).astype(jnp.bfloat16)
    return (block_out, expert_out)


def solution(mesh):
    ctx_size, exp_size = mesh.devices.shape
    split = Mesh(mesh.devices.reshape(ctx_size // 2, 2, exp_size), ("chip", "core", "exp"))
    placed = (
        P(CTX, "exp"),
        P(CTX, "exp"),
        P(CTX, None),
        P(CTX, None),
        P(CTX, "exp"),
        P("exp"),
        P("exp"),
        P(CTX, "exp"),
        P(),
        P("exp", None, CTX),
        P("exp", None, CTX),
        P("exp", CTX, None),
        P(CTX, None),
        P(CTX, None),
    )
    return jax.shard_map(
        on_device,
        mesh=split,
        in_specs=placed,
        out_specs=(P(CTX, "exp"), P(CTX, "exp")),
        check_vma=False,
    )
```

```python
import jax
import jax.numpy as jnp
from jax import lax
from jax.sharding import Mesh, PartitionSpec as P

precise = lax.Precision.HIGHEST
CTX = ("chip", "core")


def local_block(ssm_piece, key_piece, query_piece, step_piece, decay_rate, head_count):
    row_count = ssm_piece.shape[0]
    head_width = ssm_piece.shape[1] // head_count
    values = ssm_piece.astype(jnp.float32).reshape(row_count, head_count, head_width)
    key_vals = key_piece.astype(jnp.float32)
    queries = query_piece.astype(jnp.float32)
    log_steps = -step_piece * decay_rate[None, :]
    running = jnp.cumsum(log_steps, axis=0)
    scores = jnp.dot(queries, key_vals.T, precision=precise)
    causal = (jnp.arange(row_count)[:, None] >= jnp.arange(row_count)[None, :])[:, :, None]
    spacing = running[:, None, :] - running[None, :, :]
    decays = jnp.where(causal, jnp.exp(jnp.where(causal, spacing, 0.0)), 0.0)
    within = jnp.einsum("tsh,ts,shp->thp", decays, scores, values, precision=precise)
    overall = running[-1]
    fading = jnp.exp(overall[None, :] - running)
    states = jnp.einsum("sh,shp,sn->hpn", fading, values, key_vals, precision=precise)
    return (within, running, overall, states)


def route_tables(expert_ids, route_weight, experts, capacity):
    matched = expert_ids[None, :, :] == experts[:, None, None]
    member = jnp.any(matched, axis=2).astype(jnp.int32)
    gate_sum = jnp.sum(jnp.where(matched, route_weight[None, :, :], 0.0), axis=2)
    slot_index = jnp.cumsum(member, axis=1) - 1
    positions = jnp.arange(capacity, dtype=jnp.int32)
    routing = (
        (slot_index[:, None, :] == positions[None, :, None]) & (member[:, None, :] > 0)
    ).astype(jnp.float32)
    return (routing, gate_sum)


def carried_state(overall, states):
    head_count, head_width, nstate = states.shape
    rows = head_count * head_width
    high = overall.astype(jnp.bfloat16)
    low = (overall - high.astype(jnp.float32)).astype(jnp.bfloat16)
    extra = jnp.zeros((8, nstate), jnp.bfloat16)
    extra = extra.at[0, :head_count].set(high).at[1, :head_count].set(low)
    packed = jnp.concatenate([states.astype(jnp.bfloat16).reshape(rows, nstate), extra], axis=0)
    everything = lax.all_gather(packed, CTX)
    shards = everything.shape[0]
    me = lax.axis_index(CTX)
    decay_all = (
        everything[:, rows, :head_count].astype(jnp.float32)
        + everything[:, rows + 1, :head_count].astype(jnp.float32)
    )
    shard_of = jnp.arange(shards, dtype=jnp.int32)
    between = (shard_of[:, None] < shard_of[None, :]) & (shard_of[None, :] < me)
    spans = jnp.sum(jnp.where(between[:, :, None], decay_all[None, :, :], 0.0), axis=1)
    weight = jnp.where((shard_of < me)[:, None], jnp.exp(spans), 0.0)
    gathered = everything[:, :rows, :].astype(jnp.float32).reshape(
        shards, head_count, head_width, nstate
    )
    return jnp.sum(weight[:, :, None, None] * gathered, axis=0)


def on_device(
    ssm_input,
    gate_input,
    key_proj,
    query_proj,
    step_size,
    decay_rate,
    head_gain,
    residual,
    ffn_gain,
    gate_weight,
    up_weight,
    down_weight,
    expert_ids,
    route_weight,
):
    head_count = step_size.shape[1]
    row_count, channels = ssm_input.shape
    head_width = channels // head_count
    within, running, overall, states = local_block(
        ssm_input, key_proj, query_proj, step_size, decay_rate, head_count
    )
    before = carried_state(overall, states)
    carried = jnp.einsum(
        "th,hpn,tn->thp",
        jnp.exp(running),
        before,
        query_proj.astype(jnp.float32),
        precision=precise,
    )
    mixer_out = within + carried
    gated_out = mixer_out * jax.nn.silu(gate_input.astype(jnp.float32)).reshape(
        row_count, head_count, head_width
    )
    inv_rms = lax.rsqrt(jnp.mean(gated_out * gated_out, axis=2, keepdims=True) + 1e-05)
    normed = (gated_out * inv_rms).reshape(row_count, channels) * head_gain[None, :]
    block_out = (residual.astype(jnp.float32) + normed).astype(jnp.bfloat16)

    exp_count = lax.axis_size("exp")
    capacity = 3 * row_count // exp_count
    tables, gate_sum = route_tables(
        expert_ids, route_weight, jnp.arange(exp_count, dtype=jnp.int32), capacity
    )
    picked = jnp.einsum(
        "ekt,td->ekd",
        tables.astype(jnp.bfloat16),
        block_out,
        preferred_element_type=jnp.float32,
    ).astype(jnp.bfloat16)
    arrived = lax.all_to_all(picked, "exp", 0, 0)
    own_rows = jnp.transpose(arrived, (1, 0, 2)).reshape(capacity, exp_count * channels)
    widened = own_rows.astype(jnp.float32)
    chosen = (
        widened
        * lax.rsqrt(jnp.mean(widened * widened, axis=1, keepdims=True) + 1e-06)
        * ffn_gain[None, :]
    ).astype(jnp.bfloat16)

    gate_here = gate_weight[0]
    up_here = up_weight[0]
    down_here = down_weight[0]
    token_piece = lax.all_gather(chosen, ("core", "chip"), axis=0, tiled=True)
    core = lax.axis_index("core")
    half = token_piece.shape[0] // lax.axis_size("core")

    def expert_rows(which):
        rows = lax.dynamic_slice_in_dim(token_piece, which * half, half, 0)
        gate_proj = jnp.dot(rows, gate_here, preferred_element_type=jnp.float32)
        up_proj = jnp.dot(rows, up_here, preferred_element_type=jnp.float32)
        hidden = (jax.nn.silu(gate_proj) * up_proj).astype(jnp.bfloat16)
        return jnp.dot(hidden, down_here, preferred_element_type=jnp.float32)

    moved = lax.ppermute(expert_rows(1 - core).astype(jnp.bfloat16), "core", [(0, 1), (1, 0)])
    own_part = expert_rows(core)
    pair_sum = (own_part.astype(jnp.bfloat16).astype(jnp.float32) + moved.astype(jnp.float32)).astype(
        jnp.bfloat16
    )
    summed = lax.psum_scatter(pair_sum, "chip", scatter_dimension=0, tiled=True)
    outgoing = jnp.transpose(summed.reshape(capacity, exp_count, channels), (1, 0, 2))
    returned = lax.all_to_all(outgoing, "exp", 0, 0)
    weights = tables * gate_sum[:, None, :]
    expert_out = jnp.einsum(
        "ekt,ekd->td", weights, returned.astype(jnp.float32), precision=precise
    ).astype(jnp.bfloat16)
    return (block_out, expert_out)


def solution(mesh):
    ctx_size, exp_size = mesh.devices.shape
    split = Mesh(mesh.devices.reshape(ctx_size // 2, 2, exp_size), ("chip", "core", "exp"))
    placed = (
        P(CTX, "exp"),
        P(CTX, "exp"),
        P(CTX, None),
        P(CTX, None),
        P(CTX, "exp"),
        P("exp"),
        P("exp"),
        P(CTX, "exp"),
        P(),
        P("exp", None, CTX),
        P("exp", None, CTX),
        P("exp", CTX, None),
        P(CTX, None),
        P(CTX, None),
    )
    return jax.shard_map(
        on_device,
        mesh=split,
        in_specs=placed,
        out_specs=(P(CTX, "exp"), P(CTX, "exp")),
        check_vma=False,
    )
```

```python
import jax
import jax.numpy as jnp
from jax import lax
from jax.sharding import Mesh, PartitionSpec as P

precise = lax.Precision.HIGHEST
CTX = ("chip", "core")


def local_block(ssm_piece, key_piece, query_piece, step_piece, decay_rate, head_count):
    row_count = ssm_piece.shape[0]
    head_width = ssm_piece.shape[1] // head_count
    values = ssm_piece.astype(jnp.float32).reshape(row_count, head_count, head_width)
    key_vals = key_piece.astype(jnp.float32)
    queries = query_piece.astype(jnp.float32)
    log_steps = -step_piece * decay_rate[None, :]
    running = jnp.cumsum(log_steps, axis=0)
    scores = jnp.dot(queries, key_vals.T, precision=precise)
    causal = (jnp.arange(row_count)[:, None] >= jnp.arange(row_count)[None, :])[:, :, None]
    spacing = running[:, None, :] - running[None, :, :]
    decays = jnp.where(causal, jnp.exp(jnp.where(causal, spacing, 0.0)), 0.0)
    within = jnp.einsum("tsh,ts,shp->thp", decays, scores, values, precision=precise)
    overall = running[-1]
    fading = jnp.exp(overall[None, :] - running)
    states = jnp.einsum("sh,shp,sn->hpn", fading, values, key_vals, precision=precise)
    return (within, running, overall, states)


def route_tables(expert_ids, route_weight, experts, capacity):
    matched = expert_ids[None, :, :] == experts[:, None, None]
    member = jnp.any(matched, axis=2).astype(jnp.int32)
    gate_sum = jnp.sum(jnp.where(matched, route_weight[None, :, :], 0.0), axis=2)
    slot_index = jnp.cumsum(member, axis=1) - 1
    positions = jnp.arange(capacity, dtype=jnp.int32)
    routing = (
        (slot_index[:, None, :] == positions[None, :, None]) & (member[:, None, :] > 0)
    ).astype(jnp.float32)
    return (routing, gate_sum)


def carried_state(overall, states):
    head_count, head_width, nstate = states.shape
    rows = head_count * head_width
    high = overall.astype(jnp.bfloat16)
    low = (overall - high.astype(jnp.float32)).astype(jnp.bfloat16)
    extra = jnp.zeros((8, nstate), jnp.bfloat16)
    extra = extra.at[0, :head_count].set(high).at[1, :head_count].set(low)
    packed = jnp.concatenate([states.astype(jnp.bfloat16).reshape(rows, nstate), extra], axis=0)
    everything = lax.all_gather(packed, CTX)
    shards = everything.shape[0]
    me = lax.axis_index(CTX)
    decay_all = (
        everything[:, rows, :head_count].astype(jnp.float32)
        + everything[:, rows + 1, :head_count].astype(jnp.float32)
    )
    shard_of = jnp.arange(shards, dtype=jnp.int32)
    between = (shard_of[:, None] < shard_of[None, :]) & (shard_of[None, :] < me)
    spans = jnp.sum(jnp.where(between[:, :, None], decay_all[None, :, :], 0.0), axis=1)
    weight = jnp.where((shard_of < me)[:, None], jnp.exp(spans), 0.0)
    gathered = everything[:, :rows, :].astype(jnp.float32).reshape(
        shards, head_count, head_width, nstate
    )
    return jnp.sum(weight[:, :, None, None] * gathered, axis=0)


def on_device(
    ssm_input,
    gate_input,
    key_proj,
    query_proj,
    step_size,
    decay_rate,
    head_gain,
    residual,
    ffn_gain,
    gate_weight,
    up_weight,
    down_weight,
    expert_ids,
    route_weight,
):
    head_count = step_size.shape[1]
    row_count, channels = ssm_input.shape
    head_width = channels // head_count
    within, running, overall, states = local_block(
        ssm_input, key_proj, query_proj, step_size, decay_rate, head_count
    )
    before = carried_state(overall, states)
    carried = jnp.einsum(
        "th,hpn,tn->thp",
        jnp.exp(running),
        before,
        query_proj.astype(jnp.float32),
        precision=precise,
    )
    mixer_out = within + carried
    gated_out = mixer_out * jax.nn.silu(gate_input.astype(jnp.float32)).reshape(
        row_count, head_count, head_width
    )
    inv_rms = lax.rsqrt(jnp.mean(gated_out * gated_out, axis=2, keepdims=True) + 1e-05)
    normed = (gated_out * inv_rms).reshape(row_count, channels) * head_gain[None, :]
    block_out = (residual.astype(jnp.float32) + normed).astype(jnp.bfloat16)

    exp_count = lax.axis_size("exp")
    capacity = 3 * row_count // exp_count
    tables, gate_sum = route_tables(
        expert_ids, route_weight, jnp.arange(exp_count, dtype=jnp.int32), capacity
    )
    picked = jnp.einsum(
        "ekt,td->ekd",
        tables.astype(jnp.bfloat16),
        block_out,
        preferred_element_type=jnp.float32,
    ).astype(jnp.bfloat16)
    arrived = lax.all_to_all(picked, "exp", 0, 0)
    own_rows = jnp.transpose(arrived, (1, 0, 2)).reshape(capacity, exp_count * channels)
    widened = own_rows.astype(jnp.float32)
    chosen = (
        widened
        * lax.rsqrt(jnp.mean(widened * widened, axis=1, keepdims=True) + 1e-06)
        * ffn_gain[None, :]
    ).astype(jnp.bfloat16)

    gate_here = gate_weight[0]
    up_here = up_weight[0]
    down_here = down_weight[0]
    swap = [(0, 1), (1, 0)]
    gate_other = lax.ppermute(gate_here, "core", swap)
    up_other = lax.ppermute(up_here, "core", swap)
    down_other = lax.ppermute(down_here, "core", swap)
    token_piece = lax.all_gather(chosen, "chip", axis=0, tiled=True)

    def through(gate_part, up_part, down_part):
        gate_proj = jnp.dot(token_piece, gate_part, preferred_element_type=jnp.float32)
        up_proj = jnp.dot(token_piece, up_part, preferred_element_type=jnp.float32)
        hidden = (jax.nn.silu(gate_proj) * up_proj).astype(jnp.bfloat16)
        return jnp.dot(hidden, down_part, preferred_element_type=jnp.float32).astype(jnp.bfloat16)

    own_part = through(gate_here, up_here, down_here)
    other_part = through(gate_other, up_other, down_other)
    pair_sum = (own_part.astype(jnp.float32) + other_part.astype(jnp.float32)).astype(jnp.bfloat16)
    summed = lax.psum_scatter(pair_sum, "chip", scatter_dimension=0, tiled=True)
    outgoing = jnp.transpose(summed.reshape(capacity, exp_count, channels), (1, 0, 2))
    returned = lax.all_to_all(outgoing, "exp", 0, 0)
    weights = tables * gate_sum[:, None, :]
    expert_out = jnp.einsum(
        "ekt,ekd->td", weights, returned.astype(jnp.float32), precision=precise
    ).astype(jnp.bfloat16)
    return (block_out, expert_out)


def solution(mesh):
    ctx_size, exp_size = mesh.devices.shape
    split = Mesh(mesh.devices.reshape(ctx_size // 2, 2, exp_size), ("chip", "core", "exp"))
    placed = (
        P(CTX, "exp"),
        P(CTX, "exp"),
        P(CTX, None),
        P(CTX, None),
        P(CTX, "exp"),
        P("exp"),
        P("exp"),
        P(CTX, "exp"),
        P(),
        P("exp", None, CTX),
        P("exp", None, CTX),
        P("exp", CTX, None),
        P(CTX, None),
        P(CTX, None),
    )
    return jax.shard_map(
        on_device,
        mesh=split,
        in_specs=placed,
        out_specs=(P(CTX, "exp"), P(CTX, "exp")),
        check_vma=False,
    )
```

```python
import jax
import jax.numpy as jnp
from jax import lax
from jax.sharding import Mesh, PartitionSpec as P

precise = lax.Precision.HIGHEST
CTX = ("chip", "core")


def local_block(ssm_piece, key_piece, query_piece, step_piece, decay_rate, head_count):
    row_count = ssm_piece.shape[0]
    head_width = ssm_piece.shape[1] // head_count
    values = ssm_piece.astype(jnp.float32).reshape(row_count, head_count, head_width)
    key_vals = key_piece.astype(jnp.float32)
    queries = query_piece.astype(jnp.float32)
    log_steps = -step_piece * decay_rate[None, :]
    running = jnp.cumsum(log_steps, axis=0)
    scores = jnp.dot(queries, key_vals.T, precision=precise)
    causal = (jnp.arange(row_count)[:, None] >= jnp.arange(row_count)[None, :])[:, :, None]
    spacing = running[:, None, :] - running[None, :, :]
    decays = jnp.where(causal, jnp.exp(jnp.where(causal, spacing, 0.0)), 0.0)
    within = jnp.einsum("tsh,ts,shp->thp", decays, scores, values, precision=precise)
    overall = running[-1]
    fading = jnp.exp(overall[None, :] - running)
    states = jnp.einsum("sh,shp,sn->hpn", fading, values, key_vals, precision=precise)
    return (within, running, overall, states)


def route_tables(expert_ids, route_weight, experts, capacity):
    matched = expert_ids[None, :, :] == experts[:, None, None]
    member = jnp.any(matched, axis=2).astype(jnp.int32)
    gate_sum = jnp.sum(jnp.where(matched, route_weight[None, :, :], 0.0), axis=2)
    slot_index = jnp.cumsum(member, axis=1) - 1
    positions = jnp.arange(capacity, dtype=jnp.int32)
    routing = (
        (slot_index[:, None, :] == positions[None, :, None]) & (member[:, None, :] > 0)
    ).astype(jnp.float32)
    return (routing, gate_sum)


def carried_state(overall, states):
    head_count, head_width, nstate = states.shape
    rows = head_count * head_width
    high = overall.astype(jnp.bfloat16)
    low = (overall - high.astype(jnp.float32)).astype(jnp.bfloat16)
    extra = jnp.zeros((8, nstate), jnp.bfloat16)
    extra = extra.at[0, :head_count].set(high).at[1, :head_count].set(low)
    packed = jnp.concatenate([states.astype(jnp.bfloat16).reshape(rows, nstate), extra], axis=0)
    everything = lax.all_gather(packed, CTX)
    shards = everything.shape[0]
    me = lax.axis_index(CTX)
    decay_all = (
        everything[:, rows, :head_count].astype(jnp.float32)
        + everything[:, rows + 1, :head_count].astype(jnp.float32)
    )
    shard_of = jnp.arange(shards, dtype=jnp.int32)
    between = (shard_of[:, None] < shard_of[None, :]) & (shard_of[None, :] < me)
    spans = jnp.sum(jnp.where(between[:, :, None], decay_all[None, :, :], 0.0), axis=1)
    weight = jnp.where((shard_of < me)[:, None], jnp.exp(spans), 0.0)
    gathered = everything[:, :rows, :].astype(jnp.float32).reshape(
        shards, head_count, head_width, nstate
    )
    return jnp.sum(weight[:, :, None, None] * gathered, axis=0)


def on_device(
    ssm_input,
    gate_input,
    key_proj,
    query_proj,
    step_size,
    decay_rate,
    head_gain,
    residual,
    ffn_gain,
    gate_weight,
    up_weight,
    down_weight,
    expert_ids,
    route_weight,
):
    head_count = step_size.shape[1]
    row_count, channels = ssm_input.shape
    head_width = channels // head_count
    within, running, overall, states = local_block(
        ssm_input, key_proj, query_proj, step_size, decay_rate, head_count
    )
    before = carried_state(overall, states)
    carried = jnp.einsum(
        "th,hpn,tn->thp",
        jnp.exp(running),
        before,
        query_proj.astype(jnp.float32),
        precision=precise,
    )
    mixer_out = within + carried
    gated_out = mixer_out * jax.nn.silu(gate_input.astype(jnp.float32)).reshape(
        row_count, head_count, head_width
    )
    inv_rms = lax.rsqrt(jnp.mean(gated_out * gated_out, axis=2, keepdims=True) + 1e-05)
    normed = (gated_out * inv_rms).reshape(row_count, channels) * head_gain[None, :]
    block_out = (residual.astype(jnp.float32) + normed).astype(jnp.bfloat16)

    exp_count = lax.axis_size("exp")
    capacity = 3 * row_count // exp_count
    tables, gate_sum = route_tables(
        expert_ids, route_weight, jnp.arange(exp_count, dtype=jnp.int32), capacity
    )
    picked = jnp.einsum(
        "ekt,td->ekd",
        tables.astype(jnp.bfloat16),
        block_out,
        preferred_element_type=jnp.float32,
    ).astype(jnp.bfloat16)
    arrived = lax.all_to_all(picked, "exp", 0, 0)
    own_rows = jnp.transpose(arrived, (1, 0, 2)).reshape(capacity, exp_count * channels)
    widened = own_rows.astype(jnp.float32)
    chosen = (
        widened
        * lax.rsqrt(jnp.mean(widened * widened, axis=1, keepdims=True) + 1e-06)
        * ffn_gain[None, :]
    ).astype(jnp.bfloat16)

    gate_here = gate_weight[0]
    up_here = up_weight[0]
    down_here = down_weight[0]
    swap = [(0, 1), (1, 0)]
    gate_other = lax.ppermute(gate_here, "core", swap)
    up_other = lax.ppermute(up_here, "core", swap)
    down_other = lax.ppermute(down_here, "core", swap)
    token_piece = lax.all_gather(chosen, "chip", axis=0, tiled=True)

    gate_both = jnp.concatenate([gate_here, gate_other], axis=1)
    up_both = jnp.concatenate([up_here, up_other], axis=1)
    down_both = jnp.concatenate([down_here, down_other], axis=0)
    gate_proj = jnp.dot(token_piece, gate_both, preferred_element_type=jnp.float32)
    up_proj = jnp.dot(token_piece, up_both, preferred_element_type=jnp.float32)
    hidden = (jax.nn.silu(gate_proj) * up_proj).astype(jnp.bfloat16)
    pair_sum = jnp.dot(hidden, down_both, preferred_element_type=jnp.float32).astype(jnp.bfloat16)
    summed = lax.psum_scatter(pair_sum, "chip", scatter_dimension=0, tiled=True)
    outgoing = jnp.transpose(summed.reshape(capacity, exp_count, channels), (1, 0, 2))
    returned = lax.all_to_all(outgoing, "exp", 0, 0)
    weights = tables * gate_sum[:, None, :]
    expert_out = jnp.einsum(
        "ekt,ekd->td", weights, returned.astype(jnp.float32), precision=precise
    ).astype(jnp.bfloat16)
    return (block_out, expert_out)


def solution(mesh):
    ctx_size, exp_size = mesh.devices.shape
    split = Mesh(mesh.devices.reshape(ctx_size // 2, 2, exp_size), ("chip", "core", "exp"))
    placed = (
        P(CTX, "exp"),
        P(CTX, "exp"),
        P(CTX, None),
        P(CTX, None),
        P(CTX, "exp"),
        P("exp"),
        P("exp"),
        P(CTX, "exp"),
        P(),
        P("exp", None, CTX),
        P("exp", None, CTX),
        P("exp", CTX, None),
        P(CTX, None),
        P(CTX, None),
    )
    return jax.shard_map(
        on_device,
        mesh=split,
        in_specs=placed,
        out_specs=(P(CTX, "exp"), P(CTX, "exp")),
        check_vma=False,
    )
```

```python
import jax
import jax.numpy as jnp
from jax import lax
from jax.sharding import Mesh, PartitionSpec as P

precise = lax.Precision.HIGHEST
CTX = ("chip", "core")


def local_block(ssm_piece, key_piece, query_piece, step_piece, decay_rate, head_count):
    row_count = ssm_piece.shape[0]
    head_width = ssm_piece.shape[1] // head_count
    values = ssm_piece.astype(jnp.float32).reshape(row_count, head_count, head_width)
    key_vals = key_piece.astype(jnp.float32)
    queries = query_piece.astype(jnp.float32)
    log_steps = -step_piece * decay_rate[None, :]
    running = jnp.cumsum(log_steps, axis=0)
    scores = jnp.dot(queries, key_vals.T, precision=precise)
    causal = (jnp.arange(row_count)[:, None] >= jnp.arange(row_count)[None, :])[:, :, None]
    spacing = running[:, None, :] - running[None, :, :]
    decays = jnp.where(causal, jnp.exp(jnp.where(causal, spacing, 0.0)), 0.0)
    within = jnp.einsum("tsh,ts,shp->thp", decays, scores, values, precision=precise)
    overall = running[-1]
    fading = jnp.exp(overall[None, :] - running)
    states = jnp.einsum("sh,shp,sn->hpn", fading, values, key_vals, precision=precise)
    return (within, running, overall, states)


def route_tables(expert_ids, route_weight, experts, capacity):
    matched = expert_ids[None, :, :] == experts[:, None, None]
    member = jnp.any(matched, axis=2).astype(jnp.int32)
    gate_sum = jnp.sum(jnp.where(matched, route_weight[None, :, :], 0.0), axis=2)
    slot_index = jnp.cumsum(member, axis=1) - 1
    positions = jnp.arange(capacity, dtype=jnp.int32)
    routing = (
        (slot_index[:, None, :] == positions[None, :, None]) & (member[:, None, :] > 0)
    ).astype(jnp.float32)
    return (routing, gate_sum)


def carried_state(overall, states):
    head_count, head_width, nstate = states.shape
    rows = head_count * head_width
    high = overall.astype(jnp.bfloat16)
    low = (overall - high.astype(jnp.float32)).astype(jnp.bfloat16)
    extra = jnp.zeros((8, nstate), jnp.bfloat16)
    extra = extra.at[0, :head_count].set(high).at[1, :head_count].set(low)
    packed = jnp.concatenate([states.astype(jnp.bfloat16).reshape(rows, nstate), extra], axis=0)
    everything = lax.all_gather(packed, CTX)
    shards = everything.shape[0]
    me = lax.axis_index(CTX)
    decay_all = (
        everything[:, rows, :head_count].astype(jnp.float32)
        + everything[:, rows + 1, :head_count].astype(jnp.float32)
    )
    shard_of = jnp.arange(shards, dtype=jnp.int32)
    between = (shard_of[:, None] < shard_of[None, :]) & (shard_of[None, :] < me)
    spans = jnp.sum(jnp.where(between[:, :, None], decay_all[None, :, :], 0.0), axis=1)
    weight = jnp.where((shard_of < me)[:, None], jnp.exp(spans), 0.0)
    gathered = everything[:, :rows, :].reshape(shards, head_count, head_width * nstate)
    summed = jnp.einsum(
        "kh,khm->hm", weight, gathered.astype(jnp.float32), precision=precise
    )
    return summed.reshape(head_count, head_width, nstate)


def on_device(
    ssm_input,
    gate_input,
    key_proj,
    query_proj,
    step_size,
    decay_rate,
    head_gain,
    residual,
    ffn_gain,
    gate_weight,
    up_weight,
    down_weight,
    expert_ids,
    route_weight,
):
    head_count = step_size.shape[1]
    row_count, channels = ssm_input.shape
    head_width = channels // head_count
    within, running, overall, states = local_block(
        ssm_input, key_proj, query_proj, step_size, decay_rate, head_count
    )
    before = carried_state(overall, states)
    carried = jnp.einsum(
        "th,hpn,tn->thp",
        jnp.exp(running),
        before,
        query_proj.astype(jnp.float32),
        precision=precise,
    )
    mixer_out = within + carried
    gated_out = mixer_out * jax.nn.silu(gate_input.astype(jnp.float32)).reshape(
        row_count, head_count, head_width
    )
    inv_rms = lax.rsqrt(jnp.mean(gated_out * gated_out, axis=2, keepdims=True) + 1e-05)
    normed = (gated_out * inv_rms).reshape(row_count, channels) * head_gain[None, :]
    block_out = (residual.astype(jnp.float32) + normed).astype(jnp.bfloat16)

    exp_count = lax.axis_size("exp")
    capacity = 3 * row_count // exp_count
    tables, gate_sum = route_tables(
        expert_ids, route_weight, jnp.arange(exp_count, dtype=jnp.int32), capacity
    )
    picked = jnp.einsum(
        "ekt,td->ekd",
        tables.astype(jnp.bfloat16),
        block_out,
        preferred_element_type=jnp.float32,
    ).astype(jnp.bfloat16)
    arrived = lax.all_to_all(picked, "exp", 0, 0)
    own_rows = jnp.transpose(arrived, (1, 0, 2)).reshape(capacity, exp_count * channels)
    widened = own_rows.astype(jnp.float32)
    chosen = (
        widened
        * lax.rsqrt(jnp.mean(widened * widened, axis=1, keepdims=True) + 1e-06)
        * ffn_gain[None, :]
    ).astype(jnp.bfloat16)

    gate_here = gate_weight[0]
    up_here = up_weight[0]
    down_here = down_weight[0]
    swap = [(0, 1), (1, 0)]
    gate_other = lax.ppermute(gate_here, "core", swap)
    up_other = lax.ppermute(up_here, "core", swap)
    down_other = lax.ppermute(down_here, "core", swap)
    token_piece = lax.all_gather(chosen, "chip", axis=0, tiled=True)

    gate_both = jnp.concatenate([gate_here, gate_other], axis=1)
    up_both = jnp.concatenate([up_here, up_other], axis=1)
    down_both = jnp.concatenate([down_here, down_other], axis=0)
    gate_proj = jnp.dot(token_piece, gate_both, preferred_element_type=jnp.float32)
    up_proj = jnp.dot(token_piece, up_both, preferred_element_type=jnp.float32)
    hidden = (jax.nn.silu(gate_proj) * up_proj).astype(jnp.bfloat16)
    pair_sum = jnp.dot(hidden, down_both, preferred_element_type=jnp.float32).astype(jnp.bfloat16)
    summed = lax.psum_scatter(pair_sum, "chip", scatter_dimension=0, tiled=True)
    outgoing = jnp.transpose(summed.reshape(capacity, exp_count, channels), (1, 0, 2))
    returned = lax.all_to_all(outgoing, "exp", 0, 0)
    weights = tables * gate_sum[:, None, :]
    expert_out = jnp.einsum(
        "ekt,ekd->td", weights, returned.astype(jnp.float32), precision=precise
    ).astype(jnp.bfloat16)
    return (block_out, expert_out)


def solution(mesh):
    ctx_size, exp_size = mesh.devices.shape
    split = Mesh(mesh.devices.reshape(ctx_size // 2, 2, exp_size), ("chip", "core", "exp"))
    placed = (
        P(CTX, "exp"),
        P(CTX, "exp"),
        P(CTX, None),
        P(CTX, None),
        P(CTX, "exp"),
        P("exp"),
        P("exp"),
        P(CTX, "exp"),
        P(),
        P("exp", None, CTX),
        P("exp", None, CTX),
        P("exp", CTX, None),
        P(CTX, None),
        P(CTX, None),
    )
    return jax.shard_map(
        on_device,
        mesh=split,
        in_specs=placed,
        out_specs=(P(CTX, "exp"), P(CTX, "exp")),
        check_vma=False,
    )
```
